512 devices in a mesh: scen: 16 (over x, z_hi), graph: 32 (over y, z_lo, core).
Axes of the slice: x: 4, y: 4, z: 16 (z_hi: 4, z_lo: 4; z = z_hi * 4 + z_lo), core: 2. Of those that a mesh axis runs over, the one named last changes fastest.
Arguments:
- features: bfloat16 [32, 8192, 256], P('scen', 'graph'), may hold values from -6 to 6
- cotangent: bfloat16 [32, 8192, 256], P('scen', 'graph'), may hold values from -6 to 6
- adjacency_tiles: bfloat16 [32, 2, 4, 128, 128], P('graph'), may hold values from -0.25 to 0.25
- tile_columns: int32 [32, 2, 4], P('graph'), may hold values from 0 to 5, as said below
- boundary: int32 [32, 4, 128], P('graph'), may hold values from 0 to 255, as said below
- self_weight1: bfloat16 [256, 256], replicated, may hold values from -0.375 to 0.375
- message_weight1: bfloat16 [256, 256], replicated, may hold values from -0.375 to 0.375
- self_weight2: bfloat16 [256, 256], replicated, may hold values from -0.375 to 0.375
- message_weight2: bfloat16 [256, 256], replicated, may hold values from -0.375 to 0.375
Outputs:
- input_grad: bfloat16 [32, 8192, 256], P('scen', 'graph')
- self_grad1: float32 [256, 256], P('graph')
- message_grad1: float32 [256, 256], P('graph')
- self_grad2: float32 [256, 256], P('graph')
- message_grad2: float32 [256, 256], P('graph')
The draws below stay inside these ranges and needn't reach their ends.
Inputs may be any that keep to these rules, and one draw needn't show every extreme that they name: `tile_columns`: in tile row r of every partition, tile 0 has column r, tiles 1 and 2 name halo columns (2 or more), tile 3 a local column other than r; every one of the 4 halo columns is named in every partition. `boundary`: each list names 128 distinct local rows and holds rows 0 and 255.
All inputs are finite; a program needn't handle non-finite values.
Results may differ from the reference program's by a relative error of at most 0.015.
Values may be sent and summed in bfloat16 or wider, within the bound.
No kernel may reach another device: no remote copies, remote signals or barrier semaphores. Data moves between devices by JAX's collectives and lax.ppermute only.
A program may use at most 64 MiB of HBM per device.

```python
import math
import jax
import jax.numpy as jnp
from jax import lax

D = 256
NB = 256
BLOCK = 128
TPR = 4
NNB = 4
PARTITIONS = 32
NBT = 2
BUSES = 8192
SCENARIOS = 32


def draw_tile_columns(key, part):
    sub_keys = jax.random.split(key, PARTITIONS)

    def single(part_key):
        first_key, second_key = jax.random.split(part_key)
        start = jax.random.randint(first_key, (), 0, NNB)
        row_ids = jnp.arange(NBT, dtype=jnp.int32)
        other_col = (row_ids + 1 + jax.random.randint(second_key, (NBT,), 0, NBT - 1)) % NBT
        halo_low = NBT + (2 * row_ids + start) % NNB
        halo_high = NBT + (2 * row_ids + 1 + start) % NNB
        return jnp.stack([row_ids, halo_low, halo_high, other_col], axis=1).astype(jnp.int32)
    return jax.vmap(single)(sub_keys)


def draw_boundary(key, part):
    sub_keys = jax.random.split(key, PARTITIONS * NNB)

    def single(part_key):
        first_key, second_key = jax.random.split(part_key)
        middle = jax.random.permutation(first_key, NB - 2)[:BLOCK - 2] + 1
        listed = jnp.concatenate([jnp.array([0, NB - 1], jnp.int32), middle.astype(jnp.int32)])
        return jax.random.permutation(second_key, listed).astype(jnp.int32)
    return jax.vmap(single)(sub_keys).reshape(PARTITIONS, NNB, BLOCK)


def raised(values, stream_key, source, target, blocks, factor):
    owner, partner = [(jnp.arange(values.shape[axis_at]) // (values.shape[axis_at] // blocks)).reshape([-1 if axis == axis_at else 1 for axis in range(values.ndim)]) for axis_at in (source, target)]
    chosen = jax.random.permutation(stream_key, blocks)[partner]
    strong = (owner == chosen) | (owner == (partner + blocks // 2) % blocks)
    return jnp.where(strong, factor * values, values)


def shard_levels(stream_key, extent, cuts, least, top_value):
    factor_of, own = 1.0, jax.random.fold_in(stream_key, 6)
    for axis_at, parts in cuts:
        steps = jnp.exp(jax.random.uniform(jax.random.fold_in(own, axis_at), (parts,), jnp.float32, least / len(cuts), top_value / len(cuts)))
        factor_of = factor_of * jnp.repeat(steps, extent[axis_at] // parts).reshape([-1 if axis == axis_at else 1 for axis in range(len(extent))])
    return factor_of


def noise(key, shape, scale, limit, pieces=(), held_as=jnp.bfloat16):
    values = scale * jax.random.normal(key, shape, jnp.float32)
    if pieces:
        values = values * shard_levels(key, shape, pieces, -0.22, 0.18)
    return jnp.clip(values, -limit, limit).astype(held_as)


def gaussian_with(rng, dims, width, bound, cuts, heavy, kind=jnp.bfloat16):
    values = width * jax.random.normal(rng, dims, jnp.float32)
    if cuts:
        values = values * shard_levels(rng, dims, cuts, -0.22, 0.18)
    return jnp.clip(raised(values, jax.random.fold_in(rng, 3), *heavy), -bound, bound).astype(kind)


def setup_inputs(seed: int = 0) -> dict:
    keys = jax.random.split(jax.random.key(seed), 10)
    return {
        "features": gaussian_with(keys[0], (SCENARIOS, BUSES, D), 1.0, 6.0, ((0, 16), (1, 32)), (1, 2, 32, 2.75)),
        "cotangent": noise(keys[1], (SCENARIOS, BUSES, D), 1.0, 6.0, ((0, 16), (1, 32))),
        "adjacency_tiles": noise(keys[2], (PARTITIONS, NBT, TPR, BLOCK, BLOCK), (TPR * BLOCK) ** -0.5, 0.25, ((0, 32),)),
        "tile_columns": draw_tile_columns(jax.random.fold_in(keys[9], 71), 0),
        "boundary": draw_boundary(jax.random.fold_in(keys[9], 71), 0),
        "self_weight1": noise(keys[5], (D, D), D ** -0.5, 0.375),
        "message_weight1": noise(keys[6], (D, D), D ** -0.5, 0.375),
        "self_weight2": noise(keys[7], (D, D), D ** -0.5, 0.375),
        "message_weight2": noise(keys[8], (D, D), D ** -0.5, 0.375),
    }


shift_offsets = (1, 2, -1, -2)

def silu_grad(values):
    sigma = jax.nn.sigmoid(values)
    return sigma * (1.0 + values * (1.0 - sigma))

def shift_parts(blocks, offset):
    padding = jnp.zeros_like(blocks[:abs(offset)])
    if offset > 0:
        return jnp.concatenate([padding, blocks[:-offset]], axis=0)
    return jnp.concatenate([blocks[-offset:], padding], axis=0)

def forward(layer_input_rows, self_matrix, message_matrix, adjacency, columns, boundary):
    sent = jax.vmap(lambda rows_of, picks: rows_of[picks])(layer_input_rows, boundary)
    received = [shift_parts(sent[:, slot], shift_offsets[slot]) for slot in range(NNB)]
    extended = jnp.concatenate([layer_input_rows] + received, axis=1).reshape(PARTITIONS, NBT + NNB, BLOCK, D)
    picked = jax.vmap(lambda tile_set, chosen: tile_set[chosen])(extended, columns)
    neighbor_message = jnp.einsum('prjab,prjbd->prad', adjacency.astype(jnp.float32), picked.astype(jnp.float32), precision=lax.Precision.HIGHEST)
    neighbor_message = neighbor_message.reshape(PARTITIONS, NB, D).astype(jnp.bfloat16)
    preactivation = jnp.dot(layer_input_rows.reshape(-1, D), self_matrix, preferred_element_type=jnp.float32)
    preactivation = preactivation + jnp.dot(neighbor_message.reshape(-1, D), message_matrix, preferred_element_type=jnp.float32)
    return (neighbor_message, preactivation.reshape(PARTITIONS, NB, D))

def backward(layer_input_rows, neighbor_message, preactivation, out_grad, self_matrix, message_matrix, adjacency, columns, boundary):
    preactivation_gradient = (out_grad.astype(jnp.float32) * silu_grad(preactivation)).astype(jnp.bfloat16)
    flat_in = layer_input_rows.reshape(-1, D)
    flat_message = neighbor_message.reshape(-1, D)
    flat_grad = preactivation_gradient.reshape(-1, D)
    self_sum = jnp.dot(flat_in.T, flat_grad, preferred_element_type=jnp.float32)
    message_sum = jnp.dot(flat_message.T, flat_grad, preferred_element_type=jnp.float32)
    self_contribution = jnp.dot(flat_grad, self_matrix.T, preferred_element_type=jnp.float32).reshape(PARTITIONS, NB, D)
    message_grad = jnp.dot(flat_grad, message_matrix.T, preferred_element_type=jnp.float32).astype(jnp.bfloat16)
    message_grad = message_grad.reshape(PARTITIONS, NBT, BLOCK, D)
    spread = jnp.einsum('prjab,prad->prjbd', adjacency.astype(jnp.float32), message_grad.astype(jnp.float32), precision=lax.Precision.HIGHEST)
    onehot = (columns[..., None] == jnp.arange(NBT + NNB, dtype=jnp.int32)).astype(jnp.float32)
    tile_grad = jnp.einsum('prjc,prjbd->pcbd', onehot, spread, precision=lax.Precision.HIGHEST)
    accum = self_contribution + tile_grad[:, :NBT].reshape(PARTITIONS, NB, D)
    halo_grad = tile_grad[:, NBT:].astype(jnp.bfloat16)
    for slot in range(NNB):
        back = shift_parts(halo_grad[:, slot], -shift_offsets[slot])
        accum = jax.vmap(lambda target, picks, extra: target.at[picks].add(extra.astype(jnp.float32)))(accum, boundary[:, slot], back)
    return (accum.astype(jnp.bfloat16), self_sum, message_sum)

def reference(features, cotangent, adjacency_tiles, tile_columns, boundary, self_weight1, message_weight1, self_weight2, message_weight2):
    feats = features.reshape(SCENARIOS, PARTITIONS, NB, D)
    cotans = cotangent.reshape(SCENARIOS, PARTITIONS, NB, D)

    def single(carry, pair):
        feat, cotan = pair
        message1, pre1 = forward(feat, self_weight1, message_weight1, adjacency_tiles, tile_columns, boundary)
        hidden = jax.nn.silu(pre1).astype(jnp.bfloat16)
        message2, pre2 = forward(hidden, self_weight2, message_weight2, adjacency_tiles, tile_columns, boundary)
        hidden_grad, self2, msg2 = backward(hidden, message2, pre2, cotan, self_weight2, message_weight2, adjacency_tiles, tile_columns, boundary)
        in_grad, self1, msg1 = backward(feat, message1, pre1, hidden_grad, self_weight1, message_weight1, adjacency_tiles, tile_columns, boundary)
        return ((carry[0] + self1, carry[1] + msg1, carry[2] + self2, carry[3] + msg2), in_grad)
    zeros = jnp.zeros((D, D), jnp.float32)
    sums, grads_in = lax.scan(single, (zeros, zeros, zeros, zeros), (feats, cotans))
    scale = 1.0 / math.sqrt(SCENARIOS * BUSES)
    return (grads_in.reshape(SCENARIOS, BUSES, D), sums[0] * scale, sums[1] * scale, sums[2] * scale, sums[3] * scale)
```

```python
import math

import jax
import jax.numpy as jnp
from jax import lax
from jax.sharding import PartitionSpec as P

shift_offsets = (1, 2, -1, -2)
REDUCE = "pp_all"


def from_behind(value, axis, steps):
    count = lax.axis_size(axis)
    first, last = (max(0, -steps), min(count, count - steps))
    return lax.ppermute(value, axis, [(source, source + steps) for source in range(first, last)])


def silu_grad(values):
    sigma = jax.nn.sigmoid(values)
    return sigma * (1.0 + values * (1.0 - sigma))


def pass_blocks(blocks, sign):
    block_rows = blocks.shape[1] // 4
    received = [
        from_behind(blocks[:, number * block_rows : (number + 1) * block_rows], "graph", sign * shift_offsets[number])
        for number in range(4)
    ]
    return jnp.concatenate(received, axis=1)


def mm(left, right, spec):
    return jnp.einsum(spec, left, right, preferred_element_type=jnp.float32)


def forward(rows, self_matrix, message_matrix, dense, select):
    sent = mm(select, rows, "mn,snd->smd").astype(jnp.bfloat16)
    extended = jnp.concatenate([rows, pass_blocks(sent, 1)], axis=1)
    message = mm(dense, extended, "nm,smd->snd").astype(jnp.bfloat16)
    pre = mm(rows, self_matrix, "snp,pw->snw") + mm(message, message_matrix, "snp,pw->snw")
    return message, pre


def backward(rows, message, pre, out_grad, self_matrix, message_matrix, dense, select):
    bus_count = rows.shape[1]
    pre_grad = (out_grad.astype(jnp.float32) * silu_grad(pre)).astype(jnp.bfloat16)
    self_sum = mm(rows, pre_grad, "snp,snw->pw")
    message_sum = mm(message, pre_grad, "snp,snw->pw")
    accum = mm(pre_grad, self_matrix, "snf,af->sna")
    message_grad = mm(pre_grad, message_matrix, "snf,af->sna").astype(jnp.bfloat16)
    tile_grad = mm(dense, message_grad, "nm,snd->smd")
    accum = accum + tile_grad[:, :bus_count]
    halo_grad = tile_grad[:, bus_count:].astype(jnp.bfloat16)
    returned = pass_blocks(halo_grad, -1)
    accum = accum + mm(select, returned, "mn,smd->snd")
    return accum.astype(jnp.bfloat16), self_sum, message_sum


def halving_scatter(data, axis):
    count = lax.axis_size(axis)
    bits = count.bit_length() - 1
    share = data.shape[0] // count
    order = [int(format(c, f"0{bits}b")[::-1], 2) for c in range(count)]
    chunks = data.reshape(count, share, *data.shape[1:])[jnp.array(order)]
    index = lax.axis_index(axis)
    for step in range(bits):
        bit = 1 << step
        half = chunks.shape[0] // 2
        mine = (index >> step) & 1
        keep = lax.dynamic_slice_in_dim(chunks, mine * half, half, 0)
        give = lax.dynamic_slice_in_dim(chunks, (1 - mine) * half, half, 0)
        got = lax.ppermute(give, axis, [(source, source ^ bit) for source in range(count)])
        chunks = keep + got
    return chunks.reshape(share, *data.shape[1:])


def doubling_sum(data, axis):
    count = lax.axis_size(axis)
    for step in range(count.bit_length() - 1):
        bit = 1 << step
        data = data + lax.ppermute(data, axis, [(source, source ^ bit) for source in range(count)])
    return data


def reduce_grads(partials, total_rows):
    width = partials.shape[0]
    graph = lax.axis_size("graph")
    scen = lax.axis_size("scen")
    share = width // graph
    scale = 1.0 / math.sqrt(total_rows)
    if REDUCE == "allreduce":
        total = lax.psum(partials, ("scen", "graph"))
        part = lax.dynamic_slice_in_dim(total, lax.axis_index("graph") * share, share, 0)
    elif REDUCE == "scatter_then_scen":
        part = lax.psum_scatter(partials, "graph", scatter_dimension=0, tiled=True)
        part = lax.psum(part, "scen")
    elif REDUCE == "scen_then_scatter":
        part = lax.psum(partials, "scen")
        part = lax.psum_scatter(part, "graph", scatter_dimension=0, tiled=True)
    elif REDUCE == "joint_scatter":
        flat = partials.reshape(graph, scen, -1)
        piece = lax.psum_scatter(flat.reshape(graph * scen, -1), ("graph", "scen"), scatter_dimension=0, tiled=True)
        part = lax.all_gather(piece, "scen", axis=0, tiled=True).reshape(share, *partials.shape[1:])
    elif REDUCE == "alltoall":
        pieces = partials.reshape(graph, share, *partials.shape[1:])
        part = lax.all_to_all(pieces, "graph", 0, 0).sum(0)
        flat = part.reshape(scen, -1)
        flat = lax.all_to_all(flat, "scen", 0, 0).sum(0)
        part = lax.all_gather(flat, "scen", axis=0, tiled=True).reshape(part.shape)
    elif REDUCE == "pp_graph_psum_scen":
        part = lax.psum(halving_scatter(partials, "graph"), "scen")
    elif REDUCE == "pp_all":
        part = doubling_sum(halving_scatter(partials, "graph"), "scen")
    else:
        raise ValueError(REDUCE)
    return part * scale


def local(
    features,
    cotangent,
    adjacency_tiles,
    tile_columns,
    boundary,
    self_weight1,
    message_weight1,
    self_weight2,
    message_weight2,
):
    adjacency = adjacency_tiles[0]
    columns = tile_columns[0]
    row_lists = boundary[0]
    tile_rows, per_row, block_rows, _ = adjacency.shape
    bus_count = features.shape[1]
    column_count = tile_rows + 4
    onehot = (columns[:, :, None] == jnp.arange(column_count, dtype=jnp.int32)).astype(jnp.bfloat16)
    dense = jnp.einsum("rjc,rjab->racb", onehot, adjacency, preferred_element_type=jnp.float32)
    dense = dense.astype(jnp.bfloat16).reshape(tile_rows * block_rows, column_count * block_rows)
    select = (row_lists.reshape(-1)[:, None] == jnp.arange(bus_count, dtype=jnp.int32)).astype(jnp.bfloat16)

    message1, pre1 = forward(features, self_weight1, message_weight1, dense, select)
    hidden = jax.nn.silu(pre1).astype(jnp.bfloat16)
    message2, pre2 = forward(hidden, self_weight2, message_weight2, dense, select)
    hidden_grad, self2, msg2 = backward(
        hidden, message2, pre2, cotangent, self_weight2, message_weight2, dense, select
    )
    input_grad, self1, msg1 = backward(
        features, message1, pre1, hidden_grad, self_weight1, message_weight1, dense, select
    )
    total_rows = features.shape[0] * bus_count * lax.axis_size("scen") * lax.axis_size("graph")
    grads = reduce_grads(jnp.stack((self1, msg1, self2, msg2), 1), total_rows)
    return (input_grad, grads[:, 0], grads[:, 1], grads[:, 2], grads[:, 3])


def solution(mesh):
    in_specs = (
        P("scen", "graph", None),
        P("scen", "graph", None),
        P("graph", None, None, None, None),
        P("graph", None, None),
        P("graph", None, None),
        P(),
        P(),
        P(),
        P(),
    )
    out_specs = (
        P("scen", "graph", None),
        P("graph", None),
        P("graph", None),
        P("graph", None),
        P("graph", None),
    )
    return jax.shard_map(local, mesh=mesh, in_specs=in_specs, out_specs=out_specs, check_vma=False)
```

```python
import math

import jax
import jax.numpy as jnp
from jax import lax
from jax.sharding import PartitionSpec as P

shift_offsets = (1, 2, -1, -2)
REDUCE = "a2a_radix"


def from_behind(value, axis, steps):
    count = lax.axis_size(axis)
    first, last = (max(0, -steps), min(count, count - steps))
    return lax.ppermute(value, axis, [(source, source + steps) for source in range(first, last)])


def silu_grad(values):
    sigma = jax.nn.sigmoid(values)
    return sigma * (1.0 + values * (1.0 - sigma))


def pass_blocks(blocks, sign):
    block_rows = blocks.shape[1] // 4
    received = [
        from_behind(blocks[:, number * block_rows : (number + 1) * block_rows], "graph", sign * shift_offsets[number])
        for number in range(4)
    ]
    return jnp.concatenate(received, axis=1)


def mm(left, right, spec):
    return jnp.einsum(spec, left, right, preferred_element_type=jnp.float32)


def forward(rows, self_matrix, message_matrix, dense, select):
    sent = mm(select, rows, "mn,snd->smd").astype(jnp.bfloat16)
    extended = jnp.concatenate([rows, pass_blocks(sent, 1)], axis=1)
    message = mm(dense, extended, "nm,smd->snd").astype(jnp.bfloat16)
    pre = mm(rows, self_matrix, "snp,pw->snw") + mm(message, message_matrix, "snp,pw->snw")
    return message, pre


def backward(rows, message, pre, out_grad, self_matrix, message_matrix, dense, select):
    bus_count = rows.shape[1]
    pre_grad = (out_grad.astype(jnp.float32) * silu_grad(pre)).astype(jnp.bfloat16)
    self_sum = mm(rows, pre_grad, "snp,snw->pw")
    message_sum = mm(message, pre_grad, "snp,snw->pw")
    accum = mm(pre_grad, self_matrix, "snf,af->sna")
    message_grad = mm(pre_grad, message_matrix, "snf,af->sna").astype(jnp.bfloat16)
    tile_grad = mm(dense, message_grad, "nm,snd->smd")
    accum = accum + tile_grad[:, :bus_count]
    halo_grad = tile_grad[:, bus_count:].astype(jnp.bfloat16)
    returned = pass_blocks(halo_grad, -1)
    accum = accum + mm(select, returned, "mn,smd->snd")
    return accum.astype(jnp.bfloat16), self_sum, message_sum


def halving_scatter(data, axis):
    count = lax.axis_size(axis)
    bits = count.bit_length() - 1
    share = data.shape[0] // count
    order = [int(format(c, f"0{bits}b")[::-1], 2) for c in range(count)]
    chunks = data.reshape(count, share, *data.shape[1:])[jnp.array(order)]
    index = lax.axis_index(axis)
    for step in range(bits):
        bit = 1 << step
        half = chunks.shape[0] // 2
        mine = (index >> step) & 1
        keep = lax.dynamic_slice_in_dim(chunks, mine * half, half, 0)
        give = lax.dynamic_slice_in_dim(chunks, (1 - mine) * half, half, 0)
        got = lax.ppermute(give, axis, [(source, source ^ bit) for source in range(count)])
        chunks = keep + got
    return chunks.reshape(share, *data.shape[1:])


def doubling_sum(data, axis):
    count = lax.axis_size(axis)
    for step in range(count.bit_length() - 1):
        bit = 1 << step
        data = data + lax.ppermute(data, axis, [(source, source ^ bit) for source in range(count)])
    return data


def digit_of(axis, stride, size):
    return (lax.axis_index(axis) // stride) % size


def group_pairs(axis, stride, size, shift):
    count = lax.axis_size(axis)
    pairs = []
    for source in range(count):
        digit = (source // stride) % size
        pairs.append((source, source + ((digit + shift) % size - digit) * stride))
    return pairs


def group_scatter(data, axis, stride, size, dim):
    digit = digit_of(axis, stride, size)
    total = jnp.take(data, digit, axis=dim)
    for shift in range(1, size):
        give = jnp.take(data, (digit + shift) % size, axis=dim)
        total = total + lax.ppermute(give, axis, group_pairs(axis, stride, size, shift))
    return total


def group_sum(data, axis, stride, size):
    digit = digit_of(axis, stride, size)
    got = [data] + [lax.ppermute(data, axis, group_pairs(axis, stride, size, shift)) for shift in range(1, size)]
    stacked = jnp.stack(got)
    ordered = jnp.take(stacked, (digit - jnp.arange(size)) % size, axis=0)
    while ordered.shape[0] > 1:
        ordered = ordered[0::2] + ordered[1::2]
    return ordered[0]


def graph_scatter(partials):
    graph = lax.axis_size("graph")
    share = partials.shape[0] // graph
    data = partials.reshape(graph // 8, 4, 2, share, *partials.shape[1:])
    data = group_scatter(data, "graph", 1, 2, 2)
    data = group_scatter(data, "graph", 2, 4, 1)
    return group_scatter(data, "graph", 8, graph // 8, 0)


def scen_sum(data):
    data = group_sum(data, "scen", 1, 4)
    return group_sum(data, "scen", 4, lax.axis_size("scen") // 4)


def reduce_grads(partials, total_rows):
    width = partials.shape[0]
    graph = lax.axis_size("graph")
    scen = lax.axis_size("scen")
    share = width // graph
    scale = 1.0 / math.sqrt(total_rows)
    if REDUCE == "allreduce":
        total = lax.psum(partials, ("scen", "graph"))
        part = lax.dynamic_slice_in_dim(total, lax.axis_index("graph") * share, share, 0)
    elif REDUCE == "scatter_then_scen":
        part = lax.psum_scatter(partials, "graph", scatter_dimension=0, tiled=True)
        part = lax.psum(part, "scen")
    elif REDUCE == "scen_then_scatter":
        part = lax.psum(partials, "scen")
        part = lax.psum_scatter(part, "graph", scatter_dimension=0, tiled=True)
    elif REDUCE == "joint_scatter":
        flat = partials.reshape(graph, scen, -1)
        piece = lax.psum_scatter(flat.reshape(graph * scen, -1), ("graph", "scen"), scatter_dimension=0, tiled=True)
        part = lax.all_gather(piece, "scen", axis=0, tiled=True).reshape(share, *partials.shape[1:])
    elif REDUCE == "alltoall":
        pieces = partials.reshape(graph, share, *partials.shape[1:])
        part = lax.all_to_all(pieces, "graph", 0, 0).sum(0)
        flat = part.reshape(scen, -1)
        flat = lax.all_to_all(flat, "scen", 0, 0).sum(0)
        part = lax.all_gather(flat, "scen", axis=0, tiled=True).reshape(part.shape)
    elif REDUCE == "pp_graph_psum_scen":
        part = lax.psum(halving_scatter(partials, "graph"), "scen")
    elif REDUCE == "pp_all":
        part = doubling_sum(halving_scatter(partials, "graph"), "scen")
    elif REDUCE == "a2a_radix":
        pieces = partials.reshape(graph, share, *partials.shape[1:])
        part = scen_sum(lax.all_to_all(pieces, "graph", 0, 0).sum(0))
    elif REDUCE == "a2a3":
        pieces = partials.reshape(graph, share, *partials.shape[1:])
        part = lax.all_to_all(pieces, "graph", 0, 0).sum(0)
        flat = lax.all_to_all(part.reshape(scen, -1), "scen", 0, 0).sum(0)
        flat = lax.all_to_all(jnp.broadcast_to(flat, (scen, *flat.shape)), "scen", 0, 0)
        part = flat.reshape(part.shape)
    elif REDUCE == "radix":
        part = scen_sum(graph_scatter(partials))
    else:
        raise ValueError(REDUCE)
    return part * scale


def local(
    features,
    cotangent,
    adjacency_tiles,
    tile_columns,
    boundary,
    self_weight1,
    message_weight1,
    self_weight2,
    message_weight2,
):
    adjacency = adjacency_tiles[0]
    columns = tile_columns[0]
    row_lists = boundary[0]
    tile_rows, per_row, block_rows, _ = adjacency.shape
    bus_count = features.shape[1]
    column_count = tile_rows + 4
    onehot = (columns[:, :, None] == jnp.arange(column_count, dtype=jnp.int32)).astype(jnp.bfloat16)
    dense = jnp.einsum("rjc,rjab->racb", onehot, adjacency, preferred_element_type=jnp.float32)
    dense = dense.astype(jnp.bfloat16).reshape(tile_rows * block_rows, column_count * block_rows)
    select = (row_lists.reshape(-1)[:, None] == jnp.arange(bus_count, dtype=jnp.int32)).astype(jnp.bfloat16)

    message1, pre1 = forward(features, self_weight1, message_weight1, dense, select)
    hidden = jax.nn.silu(pre1).astype(jnp.bfloat16)
    message2, pre2 = forward(hidden, self_weight2, message_weight2, dense, select)
    hidden_grad, self2, msg2 = backward(
        hidden, message2, pre2, cotangent, self_weight2, message_weight2, dense, select
    )
    if REDUCE == "radix_split":
        early = graph_scatter(jnp.stack((self2, msg2), 1))
    input_grad, self1, msg1 = backward(
        features, message1, pre1, hidden_grad, self_weight1, message_weight1, dense, select
    )
    total_rows = features.shape[0] * bus_count * lax.axis_size("scen") * lax.axis_size("graph")
    if REDUCE == "radix_split":
        late = graph_scatter(jnp.stack((self1, msg1), 1))
        grads = scen_sum(jnp.concatenate((late, early), 1)) * (1.0 / math.sqrt(total_rows))
    else:
        grads = reduce_grads(jnp.stack((self1, msg1, self2, msg2), 1), total_rows)
    return (input_grad, grads[:, 0], grads[:, 1], grads[:, 2], grads[:, 3])


def solution(mesh):
    in_specs = (
        P("scen", "graph", None),
        P("scen", "graph", None),
        P("graph", None, None, None, None),
        P("graph", None, None),
        P("graph", None, None),
        P(),
        P(),
        P(),
        P(),
    )
    out_specs = (
        P("scen", "graph", None),
        P("graph", None),
        P("graph", None),
        P("graph", None),
        P("graph", None),
    )
    return jax.shard_map(local, mesh=mesh, in_specs=in_specs, out_specs=out_specs, check_vma=False)
```

```python
import math

import jax
import jax.numpy as jnp
from jax import lax
from jax.sharding import PartitionSpec as P

shift_offsets = (1, 2, -1, -2)
REDUCE = "a2a_split"


def from_behind(value, axis, steps):
    count = lax.axis_size(axis)
    first, last = (max(0, -steps), min(count, count - steps))
    return lax.ppermute(value, axis, [(source, source + steps) for source in range(first, last)])


def silu_grad(values):
    sigma = jax.nn.sigmoid(values)
    return sigma * (1.0 + values * (1.0 - sigma))


def pass_blocks(blocks, sign):
    block_rows = blocks.shape[1] // 4
    received = [
        from_behind(blocks[:, number * block_rows : (number + 1) * block_rows], "graph", sign * shift_offsets[number])
        for number in range(4)
    ]
    return jnp.concatenate(received, axis=1)


def mm(left, right, spec):
    return jnp.einsum(spec, left, right, preferred_element_type=jnp.float32)


def forward(rows, self_matrix, message_matrix, dense, select):
    sent = mm(select, rows, "mn,snd->smd").astype(jnp.bfloat16)
    extended = jnp.concatenate([rows, pass_blocks(sent, 1)], axis=1)
    message = mm(dense, extended, "nm,smd->snd").astype(jnp.bfloat16)
    pre = mm(rows, self_matrix, "snp,pw->snw") + mm(message, message_matrix, "snp,pw->snw")
    return message, pre


def backward(rows, message, pre, out_grad, self_matrix, message_matrix, dense, select):
    bus_count = rows.shape[1]
    pre_grad = (out_grad.astype(jnp.float32) * silu_grad(pre)).astype(jnp.bfloat16)
    self_sum = mm(rows, pre_grad, "snp,snw->pw")
    message_sum = mm(message, pre_grad, "snp,snw->pw")
    accum = mm(pre_grad, self_matrix, "snf,af->sna")
    message_grad = mm(pre_grad, message_matrix, "snf,af->sna").astype(jnp.bfloat16)
    tile_grad = mm(dense, message_grad, "nm,snd->smd")
    accum = accum + tile_grad[:, :bus_count]
    halo_grad = tile_grad[:, bus_count:].astype(jnp.bfloat16)
    returned = pass_blocks(halo_grad, -1)
    accum = accum + mm(select, returned, "mn,smd->snd")
    return accum.astype(jnp.bfloat16), self_sum, message_sum


def halving_scatter(data, axis):
    count = lax.axis_size(axis)
    bits = count.bit_length() - 1
    share = data.shape[0] // count
    order = [int(format(c, f"0{bits}b")[::-1], 2) for c in range(count)]
    chunks = data.reshape(count, share, *data.shape[1:])[jnp.array(order)]
    index = lax.axis_index(axis)
    for step in range(bits):
        bit = 1 << step
        half = chunks.shape[0] // 2
        mine = (index >> step) & 1
        keep = lax.dynamic_slice_in_dim(chunks, mine * half, half, 0)
        give = lax.dynamic_slice_in_dim(chunks, (1 - mine) * half, half, 0)
        got = lax.ppermute(give, axis, [(source, source ^ bit) for source in range(count)])
        chunks = keep + got
    return chunks.reshape(share, *data.shape[1:])


def doubling_sum(data, axis):
    count = lax.axis_size(axis)
    for step in range(count.bit_length() - 1):
        bit = 1 << step
        data = data + lax.ppermute(data, axis, [(source, source ^ bit) for source in range(count)])
    return data


def digit_of(axis, stride, size):
    return (lax.axis_index(axis) // stride) % size


def group_pairs(axis, stride, size, shift):
    count = lax.axis_size(axis)
    pairs = []
    for source in range(count):
        digit = (source // stride) % size
        pairs.append((source, source + ((digit + shift) % size - digit) * stride))
    return pairs


def group_scatter(data, axis, stride, size, dim):
    digit = digit_of(axis, stride, size)
    total = jnp.take(data, digit, axis=dim)
    for shift in range(1, size):
        give = jnp.take(data, (digit + shift) % size, axis=dim)
        total = total + lax.ppermute(give, axis, group_pairs(axis, stride, size, shift))
    return total


def group_sum(data, axis, stride, size):
    digit = digit_of(axis, stride, size)
    got = [data] + [lax.ppermute(data, axis, group_pairs(axis, stride, size, shift)) for shift in range(1, size)]
    stacked = jnp.stack(got)
    ordered = jnp.take(stacked, (digit - jnp.arange(size)) % size, axis=0)
    while ordered.shape[0] > 1:
        ordered = ordered[0::2] + ordered[1::2]
    return ordered[0]


def graph_scatter(partials):
    graph = lax.axis_size("graph")
    share = partials.shape[0] // graph
    data = partials.reshape(graph // 8, 4, 2, share, *partials.shape[1:])
    data = group_scatter(data, "graph", 1, 2, 2)
    data = group_scatter(data, "graph", 2, 4, 1)
    return group_scatter(data, "graph", 8, graph // 8, 0)


def scen_sum(data):
    data = group_sum(data, "scen", 1, 4)
    return group_sum(data, "scen", 4, lax.axis_size("scen") // 4)


def graph_a2a(partials):
    graph = lax.axis_size("graph")
    pieces = partials.reshape(graph, partials.shape[0] // graph, *partials.shape[1:])
    return lax.all_to_all(pieces, "graph", 0, 0).sum(0)


def reduce_grads(partials, total_rows):
    width = partials.shape[0]
    graph = lax.axis_size("graph")
    scen = lax.axis_size("scen")
    share = width // graph
    scale = 1.0 / math.sqrt(total_rows)
    if REDUCE == "allreduce":
        total = lax.psum(partials, ("scen", "graph"))
        part = lax.dynamic_slice_in_dim(total, lax.axis_index("graph") * share, share, 0)
    elif REDUCE == "scatter_then_scen":
        part = lax.psum_scatter(partials, "graph", scatter_dimension=0, tiled=True)
        part = lax.psum(part, "scen")
    elif REDUCE == "scen_then_scatter":
        part = lax.psum(partials, "scen")
        part = lax.psum_scatter(part, "graph", scatter_dimension=0, tiled=True)
    elif REDUCE == "joint_scatter":
        flat = partials.reshape(graph, scen, -1)
        piece = lax.psum_scatter(flat.reshape(graph * scen, -1), ("graph", "scen"), scatter_dimension=0, tiled=True)
        part = lax.all_gather(piece, "scen", axis=0, tiled=True).reshape(share, *partials.shape[1:])
    elif REDUCE == "alltoall":
        pieces = partials.reshape(graph, share, *partials.shape[1:])
        part = lax.all_to_all(pieces, "graph", 0, 0).sum(0)
        flat = part.reshape(scen, -1)
        flat = lax.all_to_all(flat, "scen", 0, 0).sum(0)
        part = lax.all_gather(flat, "scen", axis=0, tiled=True).reshape(part.shape)
    elif REDUCE == "pp_graph_psum_scen":
        part = lax.psum(halving_scatter(partials, "graph"), "scen")
    elif REDUCE == "pp_all":
        part = doubling_sum(halving_scatter(partials, "graph"), "scen")
    elif REDUCE == "a2a_radix":
        pieces = partials.reshape(graph, share, *partials.shape[1:])
        part = scen_sum(lax.all_to_all(pieces, "graph", 0, 0).sum(0))
    elif REDUCE == "a2a3":
        pieces = partials.reshape(graph, share, *partials.shape[1:])
        part = lax.all_to_all(pieces, "graph", 0, 0).sum(0)
        flat = lax.all_to_all(part.reshape(scen, -1), "scen", 0, 0).sum(0)
        flat = lax.all_to_all(jnp.broadcast_to(flat, (scen, *flat.shape)), "scen", 0, 0)
        part = flat.reshape(part.shape)
    elif REDUCE == "a2a_joint":
        pieces = partials.reshape(graph * scen, -1)
        piece = lax.all_to_all(pieces, ("graph", "scen"), 0, 0).sum(0)
        flat = lax.all_to_all(jnp.broadcast_to(piece, (scen, *piece.shape)), "scen", 0, 0)
        part = flat.reshape(share, *partials.shape[1:])
    elif REDUCE == "radix":
        part = scen_sum(graph_scatter(partials))
    else:
        raise ValueError(REDUCE)
    return part * scale


def local(
    features,
    cotangent,
    adjacency_tiles,
    tile_columns,
    boundary,
    self_weight1,
    message_weight1,
    self_weight2,
    message_weight2,
):
    adjacency = adjacency_tiles[0]
    columns = tile_columns[0]
    row_lists = boundary[0]
    tile_rows, per_row, block_rows, _ = adjacency.shape
    bus_count = features.shape[1]
    column_count = tile_rows + 4
    onehot = (columns[:, :, None] == jnp.arange(column_count, dtype=jnp.int32)).astype(jnp.bfloat16)
    dense = jnp.einsum("rjc,rjab->racb", onehot, adjacency, preferred_element_type=jnp.float32)
    dense = dense.astype(jnp.bfloat16).reshape(tile_rows * block_rows, column_count * block_rows)
    select = (row_lists.reshape(-1)[:, None] == jnp.arange(bus_count, dtype=jnp.int32)).astype(jnp.bfloat16)

    message1, pre1 = forward(features, self_weight1, message_weight1, dense, select)
    hidden = jax.nn.silu(pre1).astype(jnp.bfloat16)
    message2, pre2 = forward(hidden, self_weight2, message_weight2, dense, select)
    hidden_grad, self2, msg2 = backward(
        hidden, message2, pre2, cotangent, self_weight2, message_weight2, dense, select
    )
    if REDUCE == "radix_split":
        early = graph_scatter(jnp.stack((self2, msg2), 1))
    if REDUCE == "a2a_split":
        early = graph_a2a(jnp.stack((self2, msg2), 1))
    if REDUCE == "a2a_split2":
        early = scen_sum(graph_a2a(jnp.stack((self2, msg2), 1)))
    input_grad, self1, msg1 = backward(
        features, message1, pre1, hidden_grad, self_weight1, message_weight1, dense, select
    )
    total_rows = features.shape[0] * bus_count * lax.axis_size("scen") * lax.axis_size("graph")
    if REDUCE == "a2a_split2":
        late = scen_sum(graph_a2a(jnp.stack((self1, msg1), 1)))
        grads = jnp.concatenate((late, early), 1) * (1.0 / math.sqrt(total_rows))
    elif REDUCE == "a2a_split":
        late = graph_a2a(jnp.stack((self1, msg1), 1))
        grads = scen_sum(jnp.concatenate((late, early), 1)) * (1.0 / math.sqrt(total_rows))
    elif REDUCE == "radix_split":
        late = graph_scatter(jnp.stack((self1, msg1), 1))
        grads = scen_sum(jnp.concatenate((late, early), 1)) * (1.0 / math.sqrt(total_rows))
    else:
        grads = reduce_grads(jnp.stack((self1, msg1, self2, msg2), 1), total_rows)
    return (input_grad, grads[:, 0], grads[:, 1], grads[:, 2], grads[:, 3])


def solution(mesh):
    in_specs = (
        P("scen", "graph", None),
        P("scen", "graph", None),
        P("graph", None, None, None, None),
        P("graph", None, None),
        P("graph", None, None),
        P(),
        P(),
        P(),
        P(),
    )
    out_specs = (
        P("scen", "graph", None),
        P("graph", None),
        P("graph", None),
        P("graph", None),
        P("graph", None),
    )
    return jax.shard_map(local, mesh=mesh, in_specs=in_specs, out_specs=out_specs, check_vma=False)
```

```python
import math

import jax
import jax.numpy as jnp
from jax import lax
from jax.sharding import PartitionSpec as P

shift_offsets = (1, 2, -1, -2)
REDUCE = "a2a_split"
SCEN = "x_first"
HOLD = False


def from_behind(value, axis, steps):
    count = lax.axis_size(axis)
    first, last = (max(0, -steps), min(count, count - steps))
    return lax.ppermute(value, axis, [(source, source + steps) for source in range(first, last)])


def silu_grad(values):
    sigma = jax.nn.sigmoid(values)
    return sigma * (1.0 + values * (1.0 - sigma))


def pass_blocks(blocks, sign):
    block_rows = blocks.shape[1] // 4
    received = [
        from_behind(blocks[:, number * block_rows : (number + 1) * block_rows], "graph", sign * shift_offsets[number])
        for number in range(4)
    ]
    return jnp.concatenate(received, axis=1)


def mm(left, right, spec):
    return jnp.einsum(spec, left, right, preferred_element_type=jnp.float32)


def forward(rows, self_matrix, message_matrix, dense, select):
    sent = mm(select, rows, "mn,snd->smd").astype(jnp.bfloat16)
    extended = jnp.concatenate([rows, pass_blocks(sent, 1)], axis=1)
    message = mm(dense, extended, "nm,smd->snd").astype(jnp.bfloat16)
    pre = mm(rows, self_matrix, "snp,pw->snw") + mm(message, message_matrix, "snp,pw->snw")
    return message, pre


def backward(rows, message, pre, out_grad, self_matrix, message_matrix, dense, select):
    bus_count = rows.shape[1]
    pre_grad = (out_grad.astype(jnp.float32) * silu_grad(pre)).astype(jnp.bfloat16)
    self_sum = mm(rows, pre_grad, "snp,snw->pw")
    message_sum = mm(message, pre_grad, "snp,snw->pw")
    accum = mm(pre_grad, self_matrix, "snf,af->sna")
    message_grad = mm(pre_grad, message_matrix, "snf,af->sna").astype(jnp.bfloat16)
    tile_grad = mm(dense, message_grad, "nm,snd->smd")
    accum = accum + tile_grad[:, :bus_count]
    halo_grad = tile_grad[:, bus_count:].astype(jnp.bfloat16)
    returned = pass_blocks(halo_grad, -1)
    if HOLD:
        (self_sum, message_sum), returned = lax.optimization_barrier(((self_sum, message_sum), returned))
    accum = accum + mm(select, returned, "mn,smd->snd")
    return accum.astype(jnp.bfloat16), self_sum, message_sum


def halving_scatter(data, axis):
    count = lax.axis_size(axis)
    bits = count.bit_length() - 1
    share = data.shape[0] // count
    order = [int(format(c, f"0{bits}b")[::-1], 2) for c in range(count)]
    chunks = data.reshape(count, share, *data.shape[1:])[jnp.array(order)]
    index = lax.axis_index(axis)
    for step in range(bits):
        bit = 1 << step
        half = chunks.shape[0] // 2
        mine = (index >> step) & 1
        keep = lax.dynamic_slice_in_dim(chunks, mine * half, half, 0)
        give = lax.dynamic_slice_in_dim(chunks, (1 - mine) * half, half, 0)
        got = lax.ppermute(give, axis, [(source, source ^ bit) for source in range(count)])
        chunks = keep + got
    return chunks.reshape(share, *data.shape[1:])


def doubling_sum(data, axis):
    count = lax.axis_size(axis)
    for step in range(count.bit_length() - 1):
        bit = 1 << step
        data = data + lax.ppermute(data, axis, [(source, source ^ bit) for source in range(count)])
    return data


def digit_of(axis, stride, size):
    return (lax.axis_index(axis) // stride) % size


def group_pairs(axis, stride, size, shift):
    count = lax.axis_size(axis)
    pairs = []
    for source in range(count):
        digit = (source // stride) % size
        pairs.append((source, source + ((digit + shift) % size - digit) * stride))
    return pairs


def group_scatter(data, axis, stride, size, dim):
    digit = digit_of(axis, stride, size)
    total = jnp.take(data, digit, axis=dim)
    for shift in range(1, size):
        give = jnp.take(data, (digit + shift) % size, axis=dim)
        total = total + lax.ppermute(give, axis, group_pairs(axis, stride, size, shift))
    return total


def group_sum(data, axis, stride, size):
    digit = digit_of(axis, stride, size)
    got = [data] + [lax.ppermute(data, axis, group_pairs(axis, stride, size, shift)) for shift in range(1, size)]
    stacked = jnp.stack(got)
    ordered = jnp.take(stacked, (digit - jnp.arange(size)) % size, axis=0)
    while ordered.shape[0] > 1:
        ordered = ordered[0::2] + ordered[1::2]
    return ordered[0]


def graph_scatter(partials):
    graph = lax.axis_size("graph")
    share = partials.shape[0] // graph
    data = partials.reshape(graph // 8, 4, 2, share, *partials.shape[1:])
    data = group_scatter(data, "graph", 1, 2, 2)
    data = group_scatter(data, "graph", 2, 4, 1)
    return group_scatter(data, "graph", 8, graph // 8, 0)


def scen_sum(data):
    if SCEN == "doubling":
        return doubling_sum(data, "scen")
    if SCEN == "x_first":
        data = group_sum(data, "scen", 4, lax.axis_size("scen") // 4)
        return group_sum(data, "scen", 1, 4)
    data = group_sum(data, "scen", 1, 4)
    return group_sum(data, "scen", 4, lax.axis_size("scen") // 4)


def graph_a2a(partials):
    graph = lax.axis_size("graph")
    pieces = partials.reshape(graph, partials.shape[0] // graph, *partials.shape[1:])
    return lax.all_to_all(pieces, "graph", 0, 0).sum(0)


def reduce_grads(partials, total_rows):
    width = partials.shape[0]
    graph = lax.axis_size("graph")
    scen = lax.axis_size("scen")
    share = width // graph
    scale = 1.0 / math.sqrt(total_rows)
    if REDUCE == "allreduce":
        total = lax.psum(partials, ("scen", "graph"))
        part = lax.dynamic_slice_in_dim(total, lax.axis_index("graph") * share, share, 0)
    elif REDUCE == "scatter_then_scen":
        part = lax.psum_scatter(partials, "graph", scatter_dimension=0, tiled=True)
        part = lax.psum(part, "scen")
    elif REDUCE == "scen_then_scatter":
        part = lax.psum(partials, "scen")
        part = lax.psum_scatter(part, "graph", scatter_dimension=0, tiled=True)
    elif REDUCE == "joint_scatter":
        flat = partials.reshape(graph, scen, -1)
        piece = lax.psum_scatter(flat.reshape(graph * scen, -1), ("graph", "scen"), scatter_dimension=0, tiled=True)
        part = lax.all_gather(piece, "scen", axis=0, tiled=True).reshape(share, *partials.shape[1:])
    elif REDUCE == "alltoall":
        pieces = partials.reshape(graph, share, *partials.shape[1:])
        part = lax.all_to_all(pieces, "graph", 0, 0).sum(0)
        flat = part.reshape(scen, -1)
        flat = lax.all_to_all(flat, "scen", 0, 0).sum(0)
        part = lax.all_gather(flat, "scen", axis=0, tiled=True).reshape(part.shape)
    elif REDUCE == "pp_graph_psum_scen":
        part = lax.psum(halving_scatter(partials, "graph"), "scen")
    elif REDUCE == "pp_all":
        part = doubling_sum(halving_scatter(partials, "graph"), "scen")
    elif REDUCE == "a2a_radix":
        pieces = partials.reshape(graph, share, *partials.shape[1:])
        part = scen_sum(lax.all_to_all(pieces, "graph", 0, 0).sum(0))
    elif REDUCE == "a2a3":
        pieces = partials.reshape(graph, share, *partials.shape[1:])
        part = lax.all_to_all(pieces, "graph", 0, 0).sum(0)
        flat = lax.all_to_all(part.reshape(scen, -1), "scen", 0, 0).sum(0)
        flat = lax.all_to_all(jnp.broadcast_to(flat, (scen, *flat.shape)), "scen", 0, 0)
        part = flat.reshape(part.shape)
    elif REDUCE == "a2a_joint":
        pieces = partials.reshape(graph * scen, -1)
        piece = lax.all_to_all(pieces, ("graph", "scen"), 0, 0).sum(0)
        flat = lax.all_to_all(jnp.broadcast_to(piece, (scen, *piece.shape)), "scen", 0, 0)
        part = flat.reshape(share, *partials.shape[1:])
    elif REDUCE == "radix":
        part = scen_sum(graph_scatter(partials))
    else:
        raise ValueError(REDUCE)
    return part * scale


def local(
    features,
    cotangent,
    adjacency_tiles,
    tile_columns,
    boundary,
    self_weight1,
    message_weight1,
    self_weight2,
    message_weight2,
):
    adjacency = adjacency_tiles[0]
    columns = tile_columns[0]
    row_lists = boundary[0]
    tile_rows, per_row, block_rows, _ = adjacency.shape
    bus_count = features.shape[1]
    column_count = tile_rows + 4
    onehot = (columns[:, :, None] == jnp.arange(column_count, dtype=jnp.int32)).astype(jnp.bfloat16)
    dense = jnp.einsum("rjc,rjab->racb", onehot, adjacency, preferred_element_type=jnp.float32)
    dense = dense.astype(jnp.bfloat16).reshape(tile_rows * block_rows, column_count * block_rows)
    select = (row_lists.reshape(-1)[:, None] == jnp.arange(bus_count, dtype=jnp.int32)).astype(jnp.bfloat16)

    message1, pre1 = forward(features, self_weight1, message_weight1, dense, select)
    hidden = jax.nn.silu(pre1).astype(jnp.bfloat16)
    message2, pre2 = forward(hidden, self_weight2, message_weight2, dense, select)
    hidden_grad, self2, msg2 = backward(
        hidden, message2, pre2, cotangent, self_weight2, message_weight2, dense, select
    )
    if REDUCE == "radix_split":
        early = graph_scatter(jnp.stack((self2, msg2), 1))
    if REDUCE == "a2a_split":
        early = graph_a2a(jnp.stack((self2, msg2), 1))
    if REDUCE == "a2a_split2":
        early = scen_sum(graph_a2a(jnp.stack((self2, msg2), 1)))
    input_grad, self1, msg1 = backward(
        features, message1, pre1, hidden_grad, self_weight1, message_weight1, dense, select
    )
    total_rows = features.shape[0] * bus_count * lax.axis_size("scen") * lax.axis_size("graph")
    if REDUCE == "a2a_split2":
        late = scen_sum(graph_a2a(jnp.stack((self1, msg1), 1)))
        grads = jnp.concatenate((late, early), 1) * (1.0 / math.sqrt(total_rows))
    elif REDUCE == "a2a_split":
        late = graph_a2a(jnp.stack((self1, msg1), 1))
        grads = scen_sum(jnp.concatenate((late, early), 1)) * (1.0 / math.sqrt(total_rows))
    elif REDUCE == "radix_split":
        late = graph_scatter(jnp.stack((self1, msg1), 1))
        grads = scen_sum(jnp.concatenate((late, early), 1)) * (1.0 / math.sqrt(total_rows))
    else:
        grads = reduce_grads(jnp.stack((self1, msg1, self2, msg2), 1), total_rows)
    return (input_grad, grads[:, 0], grads[:, 1], grads[:, 2], grads[:, 3])


def solution(mesh):
    in_specs = (
        P("scen", "graph", None),
        P("scen", "graph", None),
        P("graph", None, None, None, None),
        P("graph", None, None),
        P("graph", None, None),
        P(),
        P(),
        P(),
        P(),
    )
    out_specs = (
        P("scen", "graph", None),
        P("graph", None),
        P("graph", None),
        P("graph", None),
        P("graph", None),
    )
    return jax.shard_map(local, mesh=mesh, in_specs=in_specs, out_specs=out_specs, check_vma=False)
```

```python
import math

import jax
import jax.numpy as jnp
from jax import lax
from jax.sharding import PartitionSpec as P

shift_offsets = (1, 2, -1, -2)
REDUCE = "a2a_split"
SCEN = "x_first"
HOLD = False


def from_behind(value, axis, steps):
    count = lax.axis_size(axis)
    first, last = (max(0, -steps), min(count, count - steps))
    return lax.ppermute(value, axis, [(source, source + steps) for source in range(first, last)])


def silu_grad(values):
    sigma = jax.nn.sigmoid(values)
    return sigma * (1.0 + values * (1.0 - sigma))


def pass_blocks(blocks, sign):
    block_rows = blocks.shape[1] // 4
    received = [
        from_behind(blocks[:, number * block_rows : (number + 1) * block_rows], "graph", sign * shift_offsets[number])
        for number in range(4)
    ]
    return jnp.concatenate(received, axis=1)


def mm(left, right, spec):
    return jnp.einsum(spec, left, right, preferred_element_type=jnp.float32)


def forward(rows, self_matrix, message_matrix, dense, select):
    sent = mm(select, rows, "mn,snd->smd").astype(jnp.bfloat16)
    extended = jnp.concatenate([rows, pass_blocks(sent, 1)], axis=1)
    message = mm(dense, extended, "nm,smd->snd").astype(jnp.bfloat16)
    pre = mm(rows, self_matrix, "snp,pw->snw") + mm(message, message_matrix, "snp,pw->snw")
    return message, pre


def backward(rows, message, pre, out_grad, self_matrix, message_matrix, dense, select):
    bus_count = rows.shape[1]
    pre_grad = (out_grad.astype(jnp.float32) * silu_grad(pre)).astype(jnp.bfloat16)
    self_sum = mm(rows, pre_grad, "snp,snw->pw")
    message_sum = mm(message, pre_grad, "snp,snw->pw")
    accum = mm(pre_grad, self_matrix, "snf,af->sna")
    message_grad = mm(pre_grad, message_matrix, "snf,af->sna").astype(jnp.bfloat16)
    tile_grad = mm(dense, message_grad, "nm,snd->smd")
    accum = accum + tile_grad[:, :bus_count]
    halo_grad = tile_grad[:, bus_count:].astype(jnp.bfloat16)
    returned = pass_blocks(halo_grad, -1)
    if HOLD:
        (self_sum, message_sum), returned = lax.optimization_barrier(((self_sum, message_sum), returned))
    accum = accum + mm(select, returned, "mn,smd->snd")
    return accum.astype(jnp.bfloat16), self_sum, message_sum


def halving_scatter(data, axis):
    count = lax.axis_size(axis)
    bits = count.bit_length() - 1
    share = data.shape[0] // count
    order = [int(format(c, f"0{bits}b")[::-1], 2) for c in range(count)]
    chunks = data.reshape(count, share, *data.shape[1:])[jnp.array(order)]
    index = lax.axis_index(axis)
    for step in range(bits):
        bit = 1 << step
        half = chunks.shape[0] // 2
        mine = (index >> step) & 1
        keep = lax.dynamic_slice_in_dim(chunks, mine * half, half, 0)
        give = lax.dynamic_slice_in_dim(chunks, (1 - mine) * half, half, 0)
        got = lax.ppermute(give, axis, [(source, source ^ bit) for source in range(count)])
        chunks = keep + got
    return chunks.reshape(share, *data.shape[1:])


def doubling_sum(data, axis):
    count = lax.axis_size(axis)
    for step in range(count.bit_length() - 1):
        bit = 1 << step
        data = data + lax.ppermute(data, axis, [(source, source ^ bit) for source in range(count)])
    return data


def digit_of(axis, stride, size):
    return (lax.axis_index(axis) // stride) % size


def group_pairs(axis, stride, size, shift):
    count = lax.axis_size(axis)
    pairs = []
    for source in range(count):
        digit = (source // stride) % size
        pairs.append((source, source + ((digit + shift) % size - digit) * stride))
    return pairs


def group_scatter(data, axis, stride, size, dim):
    digit = digit_of(axis, stride, size)
    total = jnp.take(data, digit, axis=dim)
    for shift in range(1, size):
        give = jnp.take(data, (digit + shift) % size, axis=dim)
        total = total + lax.ppermute(give, axis, group_pairs(axis, stride, size, shift))
    return total


def group_sum(data, axis, stride, size):
    digit = digit_of(axis, stride, size)
    got = [data] + [lax.ppermute(data, axis, group_pairs(axis, stride, size, shift)) for shift in range(1, size)]
    ordered = []
    for member in range(size):
        shift = (digit - member) % size
        pick = got[size - 1]
        for other in range(size - 2, -1, -1):
            pick = jnp.where(shift == other, got[other], pick)
        ordered.append(pick)
    while len(ordered) > 1:
        ordered = [ordered[i] + ordered[i + 1] for i in range(0, len(ordered), 2)]
    return ordered[0]


def graph_scatter(partials):
    graph = lax.axis_size("graph")
    share = partials.shape[0] // graph
    data = partials.reshape(graph // 8, 4, 2, share, *partials.shape[1:])
    data = group_scatter(data, "graph", 1, 2, 2)
    data = group_scatter(data, "graph", 2, 4, 1)
    return group_scatter(data, "graph", 8, graph // 8, 0)


def scen_sum(data):
    if SCEN == "doubling":
        return doubling_sum(data, "scen")
    if SCEN == "x_first":
        data = group_sum(data, "scen", 4, lax.axis_size("scen") // 4)
        return group_sum(data, "scen", 1, 4)
    data = group_sum(data, "scen", 1, 4)
    return group_sum(data, "scen", 4, lax.axis_size("scen") // 4)


def graph_a2a(partials):
    graph = lax.axis_size("graph")
    pieces = partials.reshape(graph, partials.shape[0] // graph, *partials.shape[1:])
    return lax.all_to_all(pieces, "graph", 0, 0).sum(0)


def reduce_grads(partials, total_rows):
    width = partials.shape[0]
    graph = lax.axis_size("graph")
    scen = lax.axis_size("scen")
    share = width // graph
    scale = 1.0 / math.sqrt(total_rows)
    if REDUCE == "allreduce":
        total = lax.psum(partials, ("scen", "graph"))
        part = lax.dynamic_slice_in_dim(total, lax.axis_index("graph") * share, share, 0)
    elif REDUCE == "scatter_then_scen":
        part = lax.psum_scatter(partials, "graph", scatter_dimension=0, tiled=True)
        part = lax.psum(part, "scen")
    elif REDUCE == "scen_then_scatter":
        part = lax.psum(partials, "scen")
        part = lax.psum_scatter(part, "graph", scatter_dimension=0, tiled=True)
    elif REDUCE == "joint_scatter":
        flat = partials.reshape(graph, scen, -1)
        piece = lax.psum_scatter(flat.reshape(graph * scen, -1), ("graph", "scen"), scatter_dimension=0, tiled=True)
        part = lax.all_gather(piece, "scen", axis=0, tiled=True).reshape(share, *partials.shape[1:])
    elif REDUCE == "alltoall":
        pieces = partials.reshape(graph, share, *partials.shape[1:])
        part = lax.all_to_all(pieces, "graph", 0, 0).sum(0)
        flat = part.reshape(scen, -1)
        flat = lax.all_to_all(flat, "scen", 0, 0).sum(0)
        part = lax.all_gather(flat, "scen", axis=0, tiled=True).reshape(part.shape)
    elif REDUCE == "pp_graph_psum_scen":
        part = lax.psum(halving_scatter(partials, "graph"), "scen")
    elif REDUCE == "pp_all":
        part = doubling_sum(halving_scatter(partials, "graph"), "scen")
    elif REDUCE == "a2a_radix":
        pieces = partials.reshape(graph, share, *partials.shape[1:])
        part = scen_sum(lax.all_to_all(pieces, "graph", 0, 0).sum(0))
    elif REDUCE == "a2a3":
        pieces = partials.reshape(graph, share, *partials.shape[1:])
        part = lax.all_to_all(pieces, "graph", 0, 0).sum(0)
        flat = lax.all_to_all(part.reshape(scen, -1), "scen", 0, 0).sum(0)
        flat = lax.all_to_all(jnp.broadcast_to(flat, (scen, *flat.shape)), "scen", 0, 0)
        part = flat.reshape(part.shape)
    elif REDUCE == "a2a_joint":
        pieces = partials.reshape(graph * scen, -1)
        piece = lax.all_to_all(pieces, ("graph", "scen"), 0, 0).sum(0)
        flat = lax.all_to_all(jnp.broadcast_to(piece, (scen, *piece.shape)), "scen", 0, 0)
        part = flat.reshape(share, *partials.shape[1:])
    elif REDUCE == "radix":
        part = scen_sum(graph_scatter(partials))
    else:
        raise ValueError(REDUCE)
    return part * scale


def local(
    features,
    cotangent,
    adjacency_tiles,
    tile_columns,
    boundary,
    self_weight1,
    message_weight1,
    self_weight2,
    message_weight2,
):
    adjacency = adjacency_tiles[0]
    columns = tile_columns[0]
    row_lists = boundary[0]
    tile_rows, per_row, block_rows, _ = adjacency.shape
    bus_count = features.shape[1]
    column_count = tile_rows + 4
    onehot = (columns[:, :, None] == jnp.arange(column_count, dtype=jnp.int32)).astype(jnp.bfloat16)
    dense = jnp.einsum("rjc,rjab->racb", onehot, adjacency, preferred_element_type=jnp.float32)
    dense = dense.astype(jnp.bfloat16).reshape(tile_rows * block_rows, column_count * block_rows)
    select = (row_lists.reshape(-1)[:, None] == jnp.arange(bus_count, dtype=jnp.int32)).astype(jnp.bfloat16)

    message1, pre1 = forward(features, self_weight1, message_weight1, dense, select)
    hidden = jax.nn.silu(pre1).astype(jnp.bfloat16)
    message2, pre2 = forward(hidden, self_weight2, message_weight2, dense, select)
    hidden_grad, self2, msg2 = backward(
        hidden, message2, pre2, cotangent, self_weight2, message_weight2, dense, select
    )
    if REDUCE == "radix_split":
        early = graph_scatter(jnp.stack((self2, msg2), 1))
    if REDUCE == "a2a_split":
        early = graph_a2a(jnp.stack((self2, msg2), 1))
    if REDUCE == "a2a_split2":
        early = scen_sum(graph_a2a(jnp.stack((self2, msg2), 1)))
    input_grad, self1, msg1 = backward(
        features, message1, pre1, hidden_grad, self_weight1, message_weight1, dense, select
    )
    total_rows = features.shape[0] * bus_count * lax.axis_size("scen") * lax.axis_size("graph")
    if REDUCE == "a2a_split2":
        late = scen_sum(graph_a2a(jnp.stack((self1, msg1), 1)))
        grads = jnp.concatenate((late, early), 1) * (1.0 / math.sqrt(total_rows))
    elif REDUCE == "a2a_split":
        late = graph_a2a(jnp.stack((self1, msg1), 1))
        grads = scen_sum(jnp.concatenate((late, early), 1)) * (1.0 / math.sqrt(total_rows))
    elif REDUCE == "radix_split":
        late = graph_scatter(jnp.stack((self1, msg1), 1))
        grads = scen_sum(jnp.concatenate((late, early), 1)) * (1.0 / math.sqrt(total_rows))
    else:
        grads = reduce_grads(jnp.stack((self1, msg1, self2, msg2), 1), total_rows)
    return (input_grad, grads[:, 0], grads[:, 1], grads[:, 2], grads[:, 3])


def solution(mesh):
    in_specs = (
        P("scen", "graph", None),
        P("scen", "graph", None),
        P("graph", None, None, None, None),
        P("graph", None, None),
        P("graph", None, None),
        P(),
        P(),
        P(),
        P(),
    )
    out_specs = (
        P("scen", "graph", None),
        P("graph", None),
        P("graph", None),
        P("graph", None),
        P("graph", None),
    )
    return jax.shard_map(local, mesh=mesh, in_specs=in_specs, out_specs=out_specs, check_vma=False)
```
